32 devices in a mesh: rows: 16 (over z, y, x), rep: 2 (over core).
Axes of the slice: x: 2, y: 2, z: 4, core: 2. Of those that a mesh axis runs over, the one named last changes fastest.
Arguments:
- features: bfloat16 [4096, 256], P(('rows', 'rep')), may hold values from -6 to 6
- cotangent: bfloat16 [4096, 256], P('rows'), may hold values from -6 to 6
- weight: bfloat16 [256, 256], replicated, may hold values from -0.375 to 0.375
- tile_vals: bfloat16 [32, 2, 16, 128, 128], P('rows', 'rep'), may hold values from -0.1875 to 0.1875
- tile_cols: int32 [32, 2, 16], P('rows', 'rep'), may hold values from 0 to 15, as said below
- tile_count: int32 [32, 2], P('rows', 'rep'), may hold values from 1 to 16
Outputs:
- output: bfloat16 [4096, 256], P(('rows', 'rep'))
- weight_grad: float32 [256, 256], replicated
- feature_grad: bfloat16 [4096, 256], P(('rows', 'rep'))
The draws below stay inside these ranges and needn't reach their ends.
Inputs may be any that keep to these rules, and one draw needn't show every extreme that they name: `tile_cols`: for each row tile and replica index the 16 entries are distinct.
All inputs are finite; a program needn't handle non-finite values.
Results may differ from the reference program's by a relative error of at most 0.0063.
Values may be sent and summed in bfloat16 or wider, within the bound.
No kernel may reach another device: no remote copies, remote signals or barrier semaphores. Data moves between devices by JAX's collectives and lax.ppermute only.
A program may use at most 64 MiB of HBM per device.

```python
import jax
import jax.numpy as jnp
from jax import lax

F = 256
TILE = 128
SLOTS = 16
ROWS_DEV = 128
NODES = 4096
PANEL_TILES = 2
RTILES = 32
COLQ = 16
N_REP = 2


def draw_tile_cols(key, part):
    scores = jax.random.randint(jax.random.fold_in(key, 11), (RTILES, N_REP, COLQ), 0, 1 << 20)
    scores = scores * COLQ + jnp.arange(COLQ, dtype=jnp.int32)[None, None, :]
    order = jnp.argsort(scores, axis=-1, stable=True)
    return order[:, :, :SLOTS].astype(jnp.int32)


def draw_tile_count(key, part):
    panels = RTILES // PANEL_TILES
    level = jax.random.randint(jax.random.fold_in(key, 21), (panels, 1, 1), 1, SLOTS + 1)
    jitter = jax.random.randint(jax.random.fold_in(key, 22), (panels, PANEL_TILES, N_REP), -2, 3)
    filled = jnp.clip(level + jitter, 1, SLOTS).reshape(-1)
    entries = RTILES * N_REP
    top_at = jax.random.randint(jax.random.fold_in(key, 23), (), 0, entries)
    low_at = (top_at + 1 + jax.random.randint(jax.random.fold_in(key, 24), (), 0, entries - 1)) % entries
    filled = filled.at[top_at].set(SLOTS)
    filled = filled.at[low_at].set(1)
    return filled.reshape(RTILES, N_REP).astype(jnp.int32)


def block_scale(key, extent, split, low, top_value):
    level = 1.0
    for axis_at, blocks in split:
        heights = jax.random.uniform(jax.random.fold_in(jax.random.fold_in(key, 6), axis_at), (blocks,), jnp.float32, low / len(split), top_value / len(split))
        level = level * jnp.repeat(jnp.exp(heights), extent[axis_at] // blocks).reshape((-1,) + (1,) * (len(extent) - 1 - axis_at))
    return level


def bell_draw(key, dims, width, bound, shards=(), held_as=jnp.bfloat16):
    values = jax.random.normal(key, dims, jnp.float32) * width
    if len(shards) > 0:
        values = block_scale(key, dims, shards, -0.22, 0.18) * values
    return jnp.clip(values, min=-bound, max=bound).astype(held_as)


def setup_inputs(seed: int = 0) -> dict:
    streams_of = jax.random.split(jax.random.key(seed), 7)
    return {
        "features": bell_draw(streams_of[0], (NODES, F), 1.0, 6.0, ((0, 32),)),
        "cotangent": bell_draw(streams_of[1], (NODES, F), 1.0, 6.0, ((0, 16),)),
        "weight": bell_draw(streams_of[2], (F, F), F ** -0.5, 0.375),
        "tile_vals": bell_draw(streams_of[3], (RTILES, N_REP, SLOTS, TILE, TILE), ((2.0 / (TILE * SLOTS)) ** 0.5), 0.1875, ((0, 16), (1, 2))),
        "tile_cols": draw_tile_cols(jax.random.fold_in(streams_of[6], 71), 0),
        "tile_count": draw_tile_count(jax.random.fold_in(streams_of[6], 71), 0),
    }


def global_tiles(tile_cols):
    per_block = ROWS_DEV // TILE
    replica = jnp.arange(N_REP, dtype=jnp.int32)[None, :, None]
    return ((tile_cols // per_block) * (N_REP * per_block) + replica * per_block + tile_cols % per_block).astype(jnp.int32)


def reference(features, cotangent, weight, tile_vals, tile_cols, tile_count):
    column_ids = global_tiles(tile_cols)
    slot_index = jnp.arange(SLOTS, dtype=jnp.int32)
    is_live = (slot_index[None, None, :] < tile_count[:, :, None]).astype(jnp.float32)
    feature_tiles = features.reshape(RTILES, TILE, F)

    def forward_tile(packed):
        values, indices, live_weight = packed
        picked = feature_tiles[indices].astype(jnp.float32) * live_weight[:, :, None, None]
        return jnp.einsum("rsab,rsbf->af", values.astype(jnp.float32), picked)

    aggregated = lax.map(forward_tile, (tile_vals, column_ids, is_live))
    aggregated = aggregated.reshape(NODES, F).astype(jnp.bfloat16)
    preact = jnp.dot(aggregated, weight, preferred_element_type=jnp.float32)
    sigmoid_part = jax.nn.sigmoid(preact)
    output = (preact * sigmoid_part).astype(jnp.bfloat16)
    grad_pre = (cotangent.astype(jnp.float32) * sigmoid_part * (1.0 + preact * (1.0 - sigmoid_part))).astype(jnp.bfloat16)
    weight_grad = lax.dot_general(aggregated, grad_pre, (((0,), (0,)), ((), ())), preferred_element_type=jnp.float32)
    pulled = jnp.dot(grad_pre, weight.T, preferred_element_type=jnp.float32).astype(jnp.bfloat16)
    pulled_tiles = pulled.reshape(RTILES, TILE, F)

    def backward_tile(running, packed):
        values, indices, live_weight, row_tile = packed
        products = jnp.einsum("rsab,af->rsbf", values.astype(jnp.float32), row_tile.astype(jnp.float32))
        products = products * live_weight[:, :, None, None]
        return running.at[indices.reshape(-1)].add(products.reshape(-1, TILE, F)), None

    initial = jnp.zeros((RTILES, TILE, F), jnp.float32)
    summed, unused = lax.scan(backward_tile, initial, (tile_vals, column_ids, is_live, pulled_tiles))
    return output, weight_grad, summed.reshape(NODES, F).astype(jnp.bfloat16)
```

```python
import jax
import jax.numpy as jnp
from jax import lax
from jax.sharding import PartitionSpec as P


def bit_count(n):
    return n.bit_length() - 1


def position_of(j, order):
    pos = 0
    for k, b in enumerate(order):
        pos = pos + (((j >> b) & 1) << k)
    return pos


def doubling_gather(x, axis, n, order):
    me = lax.axis_index(axis)
    buf = x[None]
    for b in order:
        pairs = [(j, j ^ (1 << b)) for j in range(n)]
        got = lax.ppermute(buf, axis, pairs)
        low = ((me >> b) & 1) == 0
        buf = jnp.where(low, jnp.concatenate([buf, got]), jnp.concatenate([got, buf]))
    return buf


def halving_scatter(buf, axis, n, order, send_dtype):
    me = lax.axis_index(axis)
    nb = bit_count(n)
    cur = buf.reshape((2,) * nb + buf.shape[1:]).astype(jnp.float32)
    axes_bits = list(range(nb - 1, -1, -1))
    for b in order:
        ax = axes_bits.index(b)
        mine = (me >> b) & 1
        keep = lax.dynamic_index_in_dim(cur, mine, ax, keepdims=False)
        send = lax.dynamic_index_in_dim(cur, 1 - mine, ax, keepdims=False)
        pairs = [(j, j ^ (1 << b)) for j in range(n)]
        got = lax.ppermute(send.astype(send_dtype), axis, pairs)
        cur = keep + got.astype(jnp.float32)
        axes_bits.pop(ax)
    return cur.reshape(buf.shape[1:])


def local(features, cotangent, weight, tile_vals, tile_cols, tile_count):
    n_rows = lax.axis_size("rows")
    n_rep = lax.axis_size("rep")
    tile = tile_vals.shape[-1]
    slots = tile_vals.shape[2]
    panel_tiles = tile_vals.shape[0]
    block_rows = features.shape[0]
    feat_width = features.shape[1]
    rep_bits = list(range(bit_count(n_rep)))
    row_bits = list(range(bit_count(n_rows)))
    me_rep = lax.axis_index("rep")

    values = tile_vals[:, 0]
    columns = tile_cols[:, 0]
    filled = tile_count[:, 0]
    col_tiles = n_rows * (block_rows // tile)

    is_live = jnp.arange(slots, dtype=jnp.int32)[None, :] < filled[:, None]
    picks = (columns[:, :, None] == jnp.arange(col_tiles, dtype=jnp.int32)[None, None, :]) & is_live[:, :, None]
    sorted_vals = jnp.einsum(
        "tsq,tsab->tqab", picks.astype(jnp.bfloat16), values, preferred_element_type=jnp.bfloat16
    )

    gather_order = row_bits[::-1]
    gathered = doubling_gather(features, "rows", n_rows, gather_order)
    natural = jnp.array([position_of(j, gather_order) for j in range(n_rows)], jnp.int32)
    gathered = jnp.take(gathered, natural, axis=0)
    partial_value = jnp.einsum(
        "tqab,qbf->taf", sorted_vals, gathered, preferred_element_type=jnp.float32
    )
    aggregated = halving_scatter(partial_value, "rep", n_rep, rep_bits, jnp.float32).astype(jnp.bfloat16)

    upstream = lax.dynamic_slice_in_dim(cotangent, me_rep * block_rows, block_rows, 0)
    preact = jnp.dot(aggregated, weight, preferred_element_type=jnp.float32)
    sigmoid_part = jax.nn.sigmoid(preact)
    output = (preact * sigmoid_part).astype(jnp.bfloat16)
    grad_pre = (
        upstream.astype(jnp.float32) * sigmoid_part * (1.0 + preact * (1.0 - sigmoid_part))
    ).astype(jnp.bfloat16)
    pulled = lax.dot_general(
        grad_pre, weight, (((1,), (1,)), ((), ())), preferred_element_type=jnp.float32
    ).astype(jnp.bfloat16)
    pulled_panel = doubling_gather(pulled, "rep", n_rep, rep_bits)
    local_weight = lax.dot_general(
        aggregated, grad_pre, (((0,), (0,)), ((), ())), preferred_element_type=jnp.float32
    )

    w_half = halving_scatter(
        local_weight.reshape(n_rep, feat_width // n_rep, feat_width), "rep", n_rep, rep_bits, jnp.float32
    )
    w_rows = w_half.shape[0] // n_rows
    w_pieces = w_half.reshape(n_rows, w_rows, feat_width)

    products = jnp.einsum(
        "tqab,taf->qbf", sorted_vals, pulled_panel, preferred_element_type=jnp.float32
    )
    products = products.reshape(n_rows, block_rows, feat_width)
    packed = jnp.concatenate([products, w_pieces], axis=1).astype(jnp.bfloat16)
    received = lax.all_to_all(packed, "rows", 0, 0, tiled=True)
    summed = jnp.sum(received.astype(jnp.float32), axis=0)
    feature_grad = summed[:block_rows].astype(jnp.bfloat16)
    w_mine = summed[block_rows:]

    w_rows_all = doubling_gather(w_mine, "rows", n_rows, row_bits)
    w_rep_all = doubling_gather(w_rows_all.reshape(-1, feat_width), "rep", n_rep, rep_bits)
    weight_grad = w_rep_all.reshape(feat_width, feat_width)
    return (output, weight_grad, feature_grad)


def solution(mesh):
    return jax.shard_map(
        local,
        mesh=mesh,
        in_specs=(
            P(("rows", "rep"), None),
            P("rows", None),
            P(),
            P("rows", "rep", None, None, None),
            P("rows", "rep", None),
            P("rows", "rep"),
        ),
        out_specs=(P(("rows", "rep"), None), P(), P(("rows", "rep"), None)),
        check_vma=False,
    )
```

```python
import jax
import jax.numpy as jnp
from jax import lax
from jax.sharding import PartitionSpec as P


def bit_count(n):
    return n.bit_length() - 1


def pairs_of(n, b):
    return [(j, j ^ (1 << b)) for j in range(n)]


def bit_slices(shape_bits, fixed):
    nb = len(shape_bits)
    return tuple(slice(*fixed.get(nb - 1 - k, (0, 2))) for k in range(nb))


def gather_contract(x_part, sorted_rel, order, n):
    nb = bit_count(n)
    t_count, a_size = sorted_rel.shape[0], sorted_rel.shape[-2]
    held = x_part.reshape((1,) * nb + x_part.shape)
    own = sorted_rel[(slice(None),) + (0,) * nb]
    acc = jnp.einsum("tab,bf->taf", own, x_part, preferred_element_type=jnp.float32)
    done = []
    for step, b in enumerate(order):
        got = lax.ppermute(held, "rows", pairs_of(n, b))
        fixed = {bb: (0, 1) for bb in range(nb) if bb not in done}
        fixed[b] = (1, 2)
        tiles = sorted_rel[(slice(None),) + bit_slices(range(nb), fixed)]
        tiles = tiles.reshape(t_count, -1, a_size, tiles.shape[-1])
        acc = acc + jnp.einsum(
            "tmab,mbf->taf", tiles, got.reshape((-1,) + x_part.shape), preferred_element_type=jnp.float32
        )
        done.append(b)
        if step + 1 < len(order):
            held = jnp.concatenate([held, got], axis=nb - 1 - b)
    return acc


def halving_scatter(rel, order, n, send_dtype):
    nb = bit_count(n)
    cur = rel
    axes_bits = list(range(nb - 1, -1, -1))
    for b in order:
        ax = axes_bits.index(b)
        keep = lax.index_in_dim(cur, 0, ax, keepdims=False)
        send = lax.index_in_dim(cur, 1, ax, keepdims=False)
        got = lax.ppermute(send.astype(send_dtype), "rows", pairs_of(n, b))
        cur = keep + got.astype(jnp.float32)
        axes_bits.pop(ax)
    return cur


def doubling_sum(x, axis, n, order):
    for b in order:
        x = x + lax.ppermute(x, axis, pairs_of(n, b))
    return x


def doubling_gather(x, axis, n):
    me = lax.axis_index(axis)
    buf = x[None]
    for b in range(bit_count(n)):
        got = lax.ppermute(buf, axis, pairs_of(n, b))
        low = ((me >> b) & 1) == 0
        buf = jnp.where(low, jnp.concatenate([buf, got]), jnp.concatenate([got, buf]))
    return buf


def local(features, cotangent, weight, tile_vals, tile_cols, tile_count):
    n_rows = lax.axis_size("rows")
    n_rep = lax.axis_size("rep")
    tile = tile_vals.shape[-1]
    slots = tile_vals.shape[2]
    panel_tiles = tile_vals.shape[0]
    block_rows = features.shape[0]
    feat_width = features.shape[1]
    nb = bit_count(n_rows)
    rep_bits = list(range(bit_count(n_rep)))
    me_rep = lax.axis_index("rep")
    me_rows = lax.axis_index("rows")

    values = tile_vals[:, 0]
    columns = tile_cols[:, 0]
    filled = tile_count[:, 0]

    is_live = jnp.arange(slots, dtype=jnp.int32)[None, :] < filled[:, None]
    relative = jnp.bitwise_xor(columns, me_rows)
    picks = (relative[:, :, None] == jnp.arange(n_rows, dtype=jnp.int32)[None, None, :]) & is_live[:, :, None]
    sorted_rel = jnp.einsum(
        "tsq,tsab->tqab", picks.astype(jnp.bfloat16), values, preferred_element_type=jnp.bfloat16
    )
    sorted_rel = sorted_rel.reshape((panel_tiles,) + (2,) * nb + (tile, tile))

    down = list(range(nb - 1, -1, -1))
    gather_orders = [down, down[:-2] + [down[-1], down[-2]]]
    width = feat_width // len(gather_orders)
    partial_value = jnp.concatenate(
        [
            gather_contract(features[:, k * width:(k + 1) * width], sorted_rel, order, n_rows)
            for k, order in enumerate(gather_orders)
        ],
        axis=-1,
    )
    panel_sum = doubling_sum(partial_value, "rep", n_rep, rep_bits)
    aggregated = panel_sum.reshape(panel_tiles * tile, feat_width).astype(jnp.bfloat16)

    preact = jnp.dot(aggregated, weight, preferred_element_type=jnp.float32)
    sigmoid_part = jax.nn.sigmoid(preact)
    output = (preact * sigmoid_part).astype(jnp.bfloat16)
    output = lax.dynamic_slice_in_dim(output, me_rep * block_rows, block_rows, 0)
    grad_pre = (
        cotangent.astype(jnp.float32) * sigmoid_part * (1.0 + preact * (1.0 - sigmoid_part))
    ).astype(jnp.bfloat16)
    pulled = lax.dot_general(
        grad_pre, weight, (((1,), (1,)), ((), ())), preferred_element_type=jnp.float32
    ).astype(jnp.bfloat16)
    local_weight = lax.dot_general(
        aggregated, grad_pre, (((0,), (0,)), ((), ())), preferred_element_type=jnp.float32
    )

    slice_rows = feat_width // n_rep
    w_slice = lax.dynamic_slice_in_dim(local_weight, me_rep * slice_rows, slice_rows, 0)
    w_order = list(range(2, nb)) + [0, 1] if nb >= 2 else list(range(nb))
    w_slice = doubling_sum(w_slice, "rows", n_rows, w_order)
    weight_grad = doubling_gather(w_slice, "rep", n_rep).reshape(feat_width, feat_width)

    pulled_tiles = pulled.reshape(panel_tiles, tile, feat_width)
    flat_rel = sorted_rel.reshape(panel_tiles, n_rows, tile, tile)
    up = list(range(nb))
    scatter_orders = [up, [up[1], up[0]] + up[2:]] if nb >= 2 else [up]
    width = feat_width // len(scatter_orders)
    pieces = []
    for k, order in enumerate(scatter_orders):
        products = jnp.einsum(
            "tqab,taf->qbf",
            flat_rel,
            pulled_tiles[:, :, k * width:(k + 1) * width],
            preferred_element_type=jnp.float32,
        )
        products = products.reshape((2,) * nb + (block_rows, width))
        pieces.append(halving_scatter(products, order, n_rows, jnp.bfloat16))
    feature_grad = jnp.concatenate(pieces, axis=-1).astype(jnp.bfloat16)
    return (output, weight_grad, feature_grad)


def solution(mesh):
    return jax.shard_map(
        local,
        mesh=mesh,
        in_specs=(
            P(("rows", "rep"), None),
            P("rows", None),
            P(),
            P("rows", "rep", None, None, None),
            P("rows", "rep", None),
            P("rows", "rep"),
        ),
        out_specs=(P(("rows", "rep"), None), P(), P(("rows", "rep"), None)),
        check_vma=False,
    )
```

```python
import jax
import jax.numpy as jnp
from jax import lax
from jax.sharding import PartitionSpec as P

GATHER_PARTS = 2
SCATTER_PARTS = 1
W_PACKED = False
PIPE_FWD = False


def bit_count(n):
    return n.bit_length() - 1


def pairs_of(n, b):
    return [(j, j ^ (1 << b)) for j in range(n)]


def bit_slices(shape_bits, fixed):
    nb = len(shape_bits)
    return tuple(slice(*fixed.get(nb - 1 - k, (0, 2))) for k in range(nb))


def gather_contract(x_part, sorted_rel, order, n):
    nb = bit_count(n)
    t_count, a_size = sorted_rel.shape[0], sorted_rel.shape[-2]
    held = x_part.reshape((1,) * nb + x_part.shape)
    acc = None
    if PIPE_FWD:
        own = sorted_rel[(slice(None),) + (0,) * nb]
        acc = jnp.einsum("tab,bf->taf", own, x_part, preferred_element_type=jnp.float32)
    done = []
    for step, b in enumerate(order):
        got = lax.ppermute(held, "rows", pairs_of(n, b))
        if not PIPE_FWD:
            held = jnp.concatenate([held, got], axis=nb - 1 - b)
            done.append(b)
            continue
        fixed = {bb: (0, 1) for bb in range(nb) if bb not in done}
        fixed[b] = (1, 2)
        tiles = sorted_rel[(slice(None),) + bit_slices(range(nb), fixed)]
        tiles = tiles.reshape(t_count, -1, a_size, tiles.shape[-1])
        acc = acc + jnp.einsum(
            "tmab,mbf->taf", tiles, got.reshape((-1,) + x_part.shape), preferred_element_type=jnp.float32
        )
        done.append(b)
        if step + 1 < len(order):
            held = jnp.concatenate([held, got], axis=nb - 1 - b)
    if not PIPE_FWD:
        every = sorted_rel.reshape(t_count, -1, a_size, sorted_rel.shape[-1])
        return jnp.einsum(
            "tmab,mbf->taf", every, held.reshape((-1,) + x_part.shape), preferred_element_type=jnp.float32
        )
    return acc


def split_words(x):
    hi = x.astype(jnp.bfloat16)
    lo = (x - hi.astype(jnp.float32)).astype(jnp.bfloat16)
    return hi, lo


def joined(hi, lo):
    return hi.astype(jnp.float32) + lo.astype(jnp.float32)


def halving_scatter(rel, order, n, send_dtype, extra=None):
    nb = bit_count(n)
    cur = rel
    axes_bits = list(range(nb - 1, -1, -1))
    width = rel.shape[-1]
    for b in order:
        ax = axes_bits.index(b)
        keep = lax.index_in_dim(cur, 0, ax, keepdims=False)
        send = lax.index_in_dim(cur, 1, ax, keepdims=False)
        if extra is None:
            got = lax.ppermute(send.astype(send_dtype), "rows", pairs_of(n, b))
        else:
            hi, lo = split_words(extra)
            flat = send.astype(send_dtype).reshape(-1, width)
            words = jnp.concatenate([flat, hi, lo])
            got_words = lax.ppermute(words, "rows", pairs_of(n, b))
            got = got_words[: flat.shape[0]].reshape(send.shape)
            rows_extra = extra.shape[0]
            got_hi = got_words[flat.shape[0]: flat.shape[0] + rows_extra]
            got_lo = got_words[flat.shape[0] + rows_extra:]
            extra = joined(hi, lo) + joined(got_hi, got_lo)
        cur = keep + got.astype(jnp.float32)
        axes_bits.pop(ax)
    return cur, extra


def doubling_sum(x, axis, n, order):
    for b in order:
        x = x + lax.ppermute(x, axis, pairs_of(n, b))
    return x


def doubling_gather(x, axis, n):
    me = lax.axis_index(axis)
    buf = x[None]
    for b in range(bit_count(n)):
        got = lax.ppermute(buf, axis, pairs_of(n, b))
        low = ((me >> b) & 1) == 0
        buf = jnp.where(low, jnp.concatenate([buf, got]), jnp.concatenate([got, buf]))
    return buf


def local(features, cotangent, weight, tile_vals, tile_cols, tile_count):
    n_rows = lax.axis_size("rows")
    n_rep = lax.axis_size("rep")
    tile = tile_vals.shape[-1]
    slots = tile_vals.shape[2]
    panel_tiles = tile_vals.shape[0]
    block_rows = features.shape[0]
    feat_width = features.shape[1]
    nb = bit_count(n_rows)
    rep_bits = list(range(bit_count(n_rep)))
    me_rep = lax.axis_index("rep")
    me_rows = lax.axis_index("rows")

    values = tile_vals[:, 0]
    columns = tile_cols[:, 0]
    filled = tile_count[:, 0]

    is_live = jnp.arange(slots, dtype=jnp.int32)[None, :] < filled[:, None]
    relative = jnp.bitwise_xor(columns, me_rows)
    picks = (relative[:, :, None] == jnp.arange(n_rows, dtype=jnp.int32)[None, None, :]) & is_live[:, :, None]
    sorted_rel = jnp.einsum(
        "tsq,tsab->tqab", picks.astype(jnp.bfloat16), values, preferred_element_type=jnp.bfloat16
    )
    sorted_rel = sorted_rel.reshape((panel_tiles,) + (2,) * nb + (tile, tile))

    down = list(range(nb - 1, -1, -1))
    gather_orders = [down, down[:-2] + [down[-1], down[-2]]][:GATHER_PARTS] if nb >= 2 else [down]
    width = feat_width // len(gather_orders)
    partial_value = jnp.concatenate(
        [
            gather_contract(features[:, k * width:(k + 1) * width], sorted_rel, order, n_rows)
            for k, order in enumerate(gather_orders)
        ],
        axis=-1,
    )
    panel_sum = doubling_sum(partial_value, "rep", n_rep, rep_bits)
    aggregated = panel_sum.reshape(panel_tiles * tile, feat_width).astype(jnp.bfloat16)

    preact = jnp.dot(aggregated, weight, preferred_element_type=jnp.float32)
    sigmoid_part = jax.nn.sigmoid(preact)
    output = (preact * sigmoid_part).astype(jnp.bfloat16)
    output = lax.dynamic_slice_in_dim(output, me_rep * block_rows, block_rows, 0)
    grad_pre = (
        cotangent.astype(jnp.float32) * sigmoid_part * (1.0 + preact * (1.0 - sigmoid_part))
    ).astype(jnp.bfloat16)
    pulled = lax.dot_general(
        grad_pre, weight, (((1,), (1,)), ((), ())), preferred_element_type=jnp.float32
    ).astype(jnp.bfloat16)
    local_weight = lax.dot_general(
        aggregated, grad_pre, (((0,), (0,)), ((), ())), preferred_element_type=jnp.float32
    )

    slice_rows = feat_width // n_rep
    w_slice = lax.dynamic_slice_in_dim(local_weight, me_rep * slice_rows, slice_rows, 0)
    if not W_PACKED:
        w_order = list(range(2, nb)) + [0, 1] if nb >= 2 else list(range(nb))
        w_slice = doubling_sum(w_slice, "rows", n_rows, w_order)

    pulled_tiles = pulled.reshape(panel_tiles, tile, feat_width)
    flat_rel = sorted_rel.reshape(panel_tiles, n_rows, tile, tile)
    up = list(range(nb))
    scatter_orders = ([up, [up[1], up[0]] + up[2:]] if nb >= 2 else [up])[:SCATTER_PARTS]
    width = feat_width // len(scatter_orders)
    pieces = []
    for k, order in enumerate(scatter_orders):
        products = jnp.einsum(
            "tqab,taf->qbf",
            flat_rel,
            pulled_tiles[:, :, k * width:(k + 1) * width],
            preferred_element_type=jnp.float32,
        )
        products = products.reshape((2,) * nb + (block_rows, width))
        extra = w_slice.reshape(-1, width) if (W_PACKED and k == 0) else None
        piece, extra = halving_scatter(products, order, n_rows, jnp.bfloat16, extra)
        if extra is not None:
            w_slice = extra.reshape(slice_rows, feat_width)
        pieces.append(piece)
    feature_grad = jnp.concatenate(pieces, axis=-1).astype(jnp.bfloat16)
    weight_grad = doubling_gather(w_slice, "rep", n_rep).reshape(feat_width, feat_width)
    return (output, weight_grad, feature_grad)


def solution(mesh):
    return jax.shard_map(
        local,
        mesh=mesh,
        in_specs=(
            P(("rows", "rep"), None),
            P("rows", None),
            P(),
            P("rows", "rep", None, None, None),
            P("rows", "rep", None),
            P("rows", "rep"),
        ),
        out_specs=(P(("rows", "rep"), None), P(), P(("rows", "rep"), None)),
        check_vma=False,
    )
```

```python
import jax
import jax.numpy as jnp
from jax import lax
from jax.sharding import PartitionSpec as P

GATHER_PARTS = 2
SCATTER_PARTS = 1
W_PACKED = False
PIPE_FWD = False
RADIX4_GATHER = True
RADIX4_SCATTER = True


def bit_count(n):
    return n.bit_length() - 1


def pairs_of(n, b):
    return [(j, j ^ (1 << b)) for j in range(n)]


def bit_slices(shape_bits, fixed):
    nb = len(shape_bits)
    return tuple(slice(*fixed.get(nb - 1 - k, (0, 2))) for k in range(nb))


def gather_contract(x_part, sorted_rel, order, n):
    nb = bit_count(n)
    t_count, a_size = sorted_rel.shape[0], sorted_rel.shape[-2]
    held = x_part.reshape((1,) * nb + x_part.shape)
    acc = None
    if PIPE_FWD:
        own = sorted_rel[(slice(None),) + (0,) * nb]
        acc = jnp.einsum("tab,bf->taf", own, x_part, preferred_element_type=jnp.float32)
    done = []
    for step, b in enumerate(order):
        got = lax.ppermute(held, "rows", pairs_of(n, b))
        if not PIPE_FWD:
            held = jnp.concatenate([held, got], axis=nb - 1 - b)
            done.append(b)
            continue
        fixed = {bb: (0, 1) for bb in range(nb) if bb not in done}
        fixed[b] = (1, 2)
        tiles = sorted_rel[(slice(None),) + bit_slices(range(nb), fixed)]
        tiles = tiles.reshape(t_count, -1, a_size, tiles.shape[-1])
        acc = acc + jnp.einsum(
            "tmab,mbf->taf", tiles, got.reshape((-1,) + x_part.shape), preferred_element_type=jnp.float32
        )
        done.append(b)
        if step + 1 < len(order):
            held = jnp.concatenate([held, got], axis=nb - 1 - b)
    if not PIPE_FWD:
        every = sorted_rel.reshape(t_count, -1, a_size, sorted_rel.shape[-1])
        return jnp.einsum(
            "tmab,mbf->taf", every, held.reshape((-1,) + x_part.shape), preferred_element_type=jnp.float32
        )
    return acc


def split_words(x):
    hi = x.astype(jnp.bfloat16)
    lo = (x - hi.astype(jnp.float32)).astype(jnp.bfloat16)
    return hi, lo


def joined(hi, lo):
    return hi.astype(jnp.float32) + lo.astype(jnp.float32)


def halving_scatter(rel, order, n, send_dtype, extra=None):
    nb = bit_count(n)
    cur = rel
    axes_bits = list(range(nb - 1, -1, -1))
    width = rel.shape[-1]
    for b in order:
        ax = axes_bits.index(b)
        keep = lax.index_in_dim(cur, 0, ax, keepdims=False)
        send = lax.index_in_dim(cur, 1, ax, keepdims=False)
        if extra is None:
            got = lax.ppermute(send.astype(send_dtype), "rows", pairs_of(n, b))
        else:
            hi, lo = split_words(extra)
            flat = send.astype(send_dtype).reshape(-1, width)
            words = jnp.concatenate([flat, hi, lo])
            got_words = lax.ppermute(words, "rows", pairs_of(n, b))
            got = got_words[: flat.shape[0]].reshape(send.shape)
            rows_extra = extra.shape[0]
            got_hi = got_words[flat.shape[0]: flat.shape[0] + rows_extra]
            got_lo = got_words[flat.shape[0] + rows_extra:]
            extra = joined(hi, lo) + joined(got_hi, got_lo)
        cur = keep + got.astype(jnp.float32)
        axes_bits.pop(ax)
    return cur, extra


def doubling_sum(x, axis, n, order):
    for b in order:
        x = x + lax.ppermute(x, axis, pairs_of(n, b))
    return x


def doubling_gather(x, axis, n):
    me = lax.axis_index(axis)
    buf = x[None]
    for b in range(bit_count(n)):
        got = lax.ppermute(buf, axis, pairs_of(n, b))
        low = ((me >> b) & 1) == 0
        buf = jnp.where(low, jnp.concatenate([buf, got]), jnp.concatenate([got, buf]))
    return buf


def bit_rounds(nb):
    rounds = []
    top = nb
    while top > 0:
        rounds.append(tuple(range(max(top - 2, 0), top)))
        top -= 2
    return rounds


def radix_gather(x, n):
    nb = bit_count(n)
    held = x.reshape((1,) * nb + x.shape)
    for bits in bit_rounds(nb):
        if len(bits) == 1:
            got = lax.ppermute(held, "rows", pairs_of(n, bits[0]))
            held = jnp.concatenate([held, got], axis=nb - 1 - bits[0])
            continue
        low, high = bits
        got_low = lax.ppermute(held, "rows", pairs_of(n, low))
        got_high = lax.ppermute(held, "rows", pairs_of(n, high))
        got_both = lax.ppermute(held, "rows", [(j, j ^ (1 << low) ^ (1 << high)) for j in range(n)])
        first = jnp.concatenate([held, got_low], axis=nb - 1 - low)
        second = jnp.concatenate([got_high, got_both], axis=nb - 1 - low)
        held = jnp.concatenate([first, second], axis=nb - 1 - high)
    return held


def radix_scatter(rel, n, send_dtype):
    nb = bit_count(n)
    cur = rel
    for bits in bit_rounds(nb)[::-1]:
        lead = cur.ndim - 2
        if len(bits) == 1:
            ax = lead - 1
            keep = lax.index_in_dim(cur, 0, ax, keepdims=False)
            send = lax.index_in_dim(cur, 1, ax, keepdims=False)
            got = lax.ppermute(send.astype(send_dtype), "rows", pairs_of(n, bits[0]))
            cur = keep + got.astype(jnp.float32)
            continue
        low, high = bits
        def part(h, l):
            return lax.index_in_dim(lax.index_in_dim(cur, h, lead - 2, keepdims=False), l, lead - 2, keepdims=False)
        keep = part(0, 0)
        got_low = lax.ppermute(part(0, 1).astype(send_dtype), "rows", pairs_of(n, low))
        got_high = lax.ppermute(part(1, 0).astype(send_dtype), "rows", pairs_of(n, high))
        got_both = lax.ppermute(
            part(1, 1).astype(send_dtype), "rows", [(j, j ^ (1 << low) ^ (1 << high)) for j in range(n)]
        )
        cur = keep + (got_low.astype(jnp.float32) + got_high.astype(jnp.float32) + got_both.astype(jnp.float32))
    return cur


def local(features, cotangent, weight, tile_vals, tile_cols, tile_count):
    n_rows = lax.axis_size("rows")
    n_rep = lax.axis_size("rep")
    tile = tile_vals.shape[-1]
    slots = tile_vals.shape[2]
    panel_tiles = tile_vals.shape[0]
    block_rows = features.shape[0]
    feat_width = features.shape[1]
    nb = bit_count(n_rows)
    rep_bits = list(range(bit_count(n_rep)))
    me_rep = lax.axis_index("rep")
    me_rows = lax.axis_index("rows")

    values = tile_vals[:, 0]
    columns = tile_cols[:, 0]
    filled = tile_count[:, 0]

    is_live = jnp.arange(slots, dtype=jnp.int32)[None, :] < filled[:, None]
    relative = jnp.bitwise_xor(columns, me_rows)
    picks = (relative[:, :, None] == jnp.arange(n_rows, dtype=jnp.int32)[None, None, :]) & is_live[:, :, None]
    sorted_rel = jnp.einsum(
        "tsq,tsab->tqab", picks.astype(jnp.bfloat16), values, preferred_element_type=jnp.bfloat16
    )
    sorted_rel = sorted_rel.reshape((panel_tiles,) + (2,) * nb + (tile, tile))

    if RADIX4_GATHER:
        held = radix_gather(features, n_rows)
        every = sorted_rel.reshape(panel_tiles, n_rows, tile, tile)
        partial_value = jnp.einsum(
            "tqab,qbf->taf", every, held.reshape(n_rows, block_rows, feat_width),
            preferred_element_type=jnp.float32,
        )
    else:
        down = list(range(nb - 1, -1, -1))
        gather_orders = [down, down[:-2] + [down[-1], down[-2]]][:GATHER_PARTS] if nb >= 2 else [down]
        width = feat_width // len(gather_orders)
        partial_value = jnp.concatenate(
            [
                gather_contract(features[:, k * width:(k + 1) * width], sorted_rel, order, n_rows)
                for k, order in enumerate(gather_orders)
            ],
            axis=-1,
        )
    panel_sum = doubling_sum(partial_value, "rep", n_rep, rep_bits)
    aggregated = panel_sum.reshape(panel_tiles * tile, feat_width).astype(jnp.bfloat16)

    preact = jnp.dot(aggregated, weight, preferred_element_type=jnp.float32)
    sigmoid_part = jax.nn.sigmoid(preact)
    output = (preact * sigmoid_part).astype(jnp.bfloat16)
    output = lax.dynamic_slice_in_dim(output, me_rep * block_rows, block_rows, 0)
    grad_pre = (
        cotangent.astype(jnp.float32) * sigmoid_part * (1.0 + preact * (1.0 - sigmoid_part))
    ).astype(jnp.bfloat16)
    pulled = lax.dot_general(
        grad_pre, weight, (((1,), (1,)), ((), ())), preferred_element_type=jnp.float32
    ).astype(jnp.bfloat16)
    local_weight = lax.dot_general(
        aggregated, grad_pre, (((0,), (0,)), ((), ())), preferred_element_type=jnp.float32
    )

    slice_rows = feat_width // n_rep
    w_slice = lax.dynamic_slice_in_dim(local_weight, me_rep * slice_rows, slice_rows, 0)
    if not W_PACKED:
        w_order = list(range(2, nb)) + [0, 1] if nb >= 2 else list(range(nb))
        w_slice = doubling_sum(w_slice, "rows", n_rows, w_order)

    pulled_tiles = pulled.reshape(panel_tiles, tile, feat_width)
    flat_rel = sorted_rel.reshape(panel_tiles, n_rows, tile, tile)
    up = list(range(nb))
    scatter_orders = ([up, [up[1], up[0]] + up[2:]] if nb >= 2 else [up])[:SCATTER_PARTS]
    if RADIX4_SCATTER:
        scatter_orders = [None]
    width = feat_width // len(scatter_orders)
    pieces = []
    for k, order in enumerate(scatter_orders):
        products = jnp.einsum(
            "tqab,taf->qbf",
            flat_rel,
            pulled_tiles[:, :, k * width:(k + 1) * width],
            preferred_element_type=jnp.float32,
        )
        products = products.reshape((2,) * nb + (block_rows, width))
        if order is None:
            pieces.append(radix_scatter(products, n_rows, jnp.bfloat16))
            continue
        extra = w_slice.reshape(-1, width) if (W_PACKED and k == 0) else None
        piece, extra = halving_scatter(products, order, n_rows, jnp.bfloat16, extra)
        if extra is not None:
            w_slice = extra.reshape(slice_rows, feat_width)
        pieces.append(piece)
    feature_grad = jnp.concatenate(pieces, axis=-1).astype(jnp.bfloat16)
    weight_grad = doubling_gather(w_slice, "rep", n_rep).reshape(feat_width, feat_width)
    return (output, weight_grad, feature_grad)


def solution(mesh):
    return jax.shard_map(
        local,
        mesh=mesh,
        in_specs=(
            P(("rows", "rep"), None),
            P("rows", None),
            P(),
            P("rows", "rep", None, None, None),
            P("rows", "rep", None),
            P("rows", "rep"),
        ),
        out_specs=(P(("rows", "rep"), None), P(), P(("rows", "rep"), None)),
        check_vma=False,
    )
```

```python
import jax
import jax.numpy as jnp
from jax import lax
from jax.sharding import PartitionSpec as P

GATHER_PARTS = 2
SCATTER_PARTS = 1
W_PACKED = False
PIPE_FWD = False
RADIX4_GATHER = True
RADIX4_SCATTER = True
PAIRED_BACKWARD = True
TIE_ROUNDS = False


def bit_count(n):
    return n.bit_length() - 1


def pairs_of(n, b):
    return [(j, j ^ (1 << b)) for j in range(n)]


def bit_slices(shape_bits, fixed):
    nb = len(shape_bits)
    return tuple(slice(*fixed.get(nb - 1 - k, (0, 2))) for k in range(nb))


def gather_contract(x_part, sorted_rel, order, n):
    nb = bit_count(n)
    t_count, a_size = sorted_rel.shape[0], sorted_rel.shape[-2]
    held = x_part.reshape((1,) * nb + x_part.shape)
    acc = None
    if PIPE_FWD:
        own = sorted_rel[(slice(None),) + (0,) * nb]
        acc = jnp.einsum("tab,bf->taf", own, x_part, preferred_element_type=jnp.float32)
    done = []
    for step, b in enumerate(order):
        got = lax.ppermute(held, "rows", pairs_of(n, b))
        if not PIPE_FWD:
            held = jnp.concatenate([held, got], axis=nb - 1 - b)
            done.append(b)
            continue
        fixed = {bb: (0, 1) for bb in range(nb) if bb not in done}
        fixed[b] = (1, 2)
        tiles = sorted_rel[(slice(None),) + bit_slices(range(nb), fixed)]
        tiles = tiles.reshape(t_count, -1, a_size, tiles.shape[-1])
        acc = acc + jnp.einsum(
            "tmab,mbf->taf", tiles, got.reshape((-1,) + x_part.shape), preferred_element_type=jnp.float32
        )
        done.append(b)
        if step + 1 < len(order):
            held = jnp.concatenate([held, got], axis=nb - 1 - b)
    if not PIPE_FWD:
        every = sorted_rel.reshape(t_count, -1, a_size, sorted_rel.shape[-1])
        return jnp.einsum(
            "tmab,mbf->taf", every, held.reshape((-1,) + x_part.shape), preferred_element_type=jnp.float32
        )
    return acc


def split_words(x):
    hi = x.astype(jnp.bfloat16)
    lo = (x - hi.astype(jnp.float32)).astype(jnp.bfloat16)
    return hi, lo


def joined(hi, lo):
    return hi.astype(jnp.float32) + lo.astype(jnp.float32)


def halving_scatter(rel, order, n, send_dtype, extra=None):
    nb = bit_count(n)
    cur = rel
    axes_bits = list(range(nb - 1, -1, -1))
    width = rel.shape[-1]
    for b in order:
        ax = axes_bits.index(b)
        keep = lax.index_in_dim(cur, 0, ax, keepdims=False)
        send = lax.index_in_dim(cur, 1, ax, keepdims=False)
        if extra is None:
            got = lax.ppermute(send.astype(send_dtype), "rows", pairs_of(n, b))
        else:
            hi, lo = split_words(extra)
            flat = send.astype(send_dtype).reshape(-1, width)
            words = jnp.concatenate([flat, hi, lo])
            got_words = lax.ppermute(words, "rows", pairs_of(n, b))
            got = got_words[: flat.shape[0]].reshape(send.shape)
            rows_extra = extra.shape[0]
            got_hi = got_words[flat.shape[0]: flat.shape[0] + rows_extra]
            got_lo = got_words[flat.shape[0] + rows_extra:]
            extra = joined(hi, lo) + joined(got_hi, got_lo)
        cur = keep + got.astype(jnp.float32)
        axes_bits.pop(ax)
    return cur, extra


def doubling_sum(x, axis, n, order):
    for b in order:
        x = x + lax.ppermute(x, axis, pairs_of(n, b))
    return x


def doubling_gather(x, axis, n):
    me = lax.axis_index(axis)
    buf = x[None]
    for b in range(bit_count(n)):
        got = lax.ppermute(buf, axis, pairs_of(n, b))
        low = ((me >> b) & 1) == 0
        buf = jnp.where(low, jnp.concatenate([buf, got]), jnp.concatenate([got, buf]))
    return buf


def bit_rounds(nb):
    rounds = []
    top = nb
    while top > 0:
        rounds.append(tuple(range(max(top - 2, 0), top)))
        top -= 2
    return rounds


def radix_gather(x, n):
    nb = bit_count(n)
    held = x.reshape((1,) * nb + x.shape)
    for bits in bit_rounds(nb):
        if len(bits) == 1:
            got = lax.ppermute(held, "rows", pairs_of(n, bits[0]))
            held = jnp.concatenate([held, got], axis=nb - 1 - bits[0])
            continue
        low, high = bits
        got_low = lax.ppermute(held, "rows", pairs_of(n, low))
        got_high = lax.ppermute(held, "rows", pairs_of(n, high))
        got_both = lax.ppermute(held, "rows", [(j, j ^ (1 << low) ^ (1 << high)) for j in range(n)])
        first = jnp.concatenate([held, got_low], axis=nb - 1 - low)
        second = jnp.concatenate([got_high, got_both], axis=nb - 1 - low)
        held = jnp.concatenate([first, second], axis=nb - 1 - high)
    return held


def radix_scatter(rel, n, send_dtype):
    nb = bit_count(n)
    cur = rel
    for bits in bit_rounds(nb)[::-1]:
        lead = cur.ndim - 2
        if len(bits) == 1:
            ax = lead - 1
            keep = lax.index_in_dim(cur, 0, ax, keepdims=False)
            send = lax.index_in_dim(cur, 1, ax, keepdims=False)
            got = lax.ppermute(send.astype(send_dtype), "rows", pairs_of(n, bits[0]))
            cur = keep + got.astype(jnp.float32)
            continue
        low, high = bits
        def part(h, l):
            return lax.index_in_dim(lax.index_in_dim(cur, h, lead - 2, keepdims=False), l, lead - 2, keepdims=False)
        keep = part(0, 0)
        got_low = lax.ppermute(part(0, 1).astype(send_dtype), "rows", pairs_of(n, low))
        got_high = lax.ppermute(part(1, 0).astype(send_dtype), "rows", pairs_of(n, high))
        got_both = lax.ppermute(
            part(1, 1).astype(send_dtype), "rows", [(j, j ^ (1 << low) ^ (1 << high)) for j in range(n)]
        )
        cur = keep + (got_low.astype(jnp.float32) + got_high.astype(jnp.float32) + got_both.astype(jnp.float32))
    return cur


def scatter_round(cur, bits, n, send_dtype):
    lead = cur.ndim - 2
    if len(bits) == 1:
        keep = lax.index_in_dim(cur, 0, lead - 1, keepdims=False)
        send = lax.index_in_dim(cur, 1, lead - 1, keepdims=False)
        return keep + lax.ppermute(send.astype(send_dtype), "rows", pairs_of(n, bits[0])).astype(jnp.float32)
    low, high = bits

    def part(h, l):
        return lax.index_in_dim(lax.index_in_dim(cur, h, lead - 2, keepdims=False), l, lead - 2, keepdims=False)

    got_low = lax.ppermute(part(0, 1).astype(send_dtype), "rows", pairs_of(n, low))
    got_high = lax.ppermute(part(1, 0).astype(send_dtype), "rows", pairs_of(n, high))
    got_both = lax.ppermute(
        part(1, 1).astype(send_dtype), "rows", [(j, j ^ (1 << low) ^ (1 << high)) for j in range(n)]
    )
    return part(0, 0) + (got_low.astype(jnp.float32) + got_high.astype(jnp.float32) + got_both.astype(jnp.float32))


def sum_round(w, bits, n):
    if len(bits) == 1:
        return w + lax.ppermute(w, "rows", pairs_of(n, bits[0]))
    low, high = bits
    got_low = lax.ppermute(w, "rows", pairs_of(n, low))
    got_high = lax.ppermute(w, "rows", pairs_of(n, high))
    got_both = lax.ppermute(w, "rows", [(j, j ^ (1 << low) ^ (1 << high)) for j in range(n)])
    return (w + got_low) + (got_high + got_both)


def paired_backward(rel, w, n, send_dtype):
    rounds = bit_rounds(bit_count(n))
    cur = rel
    for k, bits in enumerate(rounds[::-1]):
        cur = scatter_round(cur, bits, n, send_dtype)
        w = sum_round(w, rounds[k], n)
        if TIE_ROUNDS:
            cur, w = lax.optimization_barrier((cur, w))
    return cur, w


def local(features, cotangent, weight, tile_vals, tile_cols, tile_count):
    n_rows = lax.axis_size("rows")
    n_rep = lax.axis_size("rep")
    tile = tile_vals.shape[-1]
    slots = tile_vals.shape[2]
    panel_tiles = tile_vals.shape[0]
    block_rows = features.shape[0]
    feat_width = features.shape[1]
    nb = bit_count(n_rows)
    rep_bits = list(range(bit_count(n_rep)))
    me_rep = lax.axis_index("rep")
    me_rows = lax.axis_index("rows")

    values = tile_vals[:, 0]
    columns = tile_cols[:, 0]
    filled = tile_count[:, 0]

    is_live = jnp.arange(slots, dtype=jnp.int32)[None, :] < filled[:, None]
    relative = jnp.bitwise_xor(columns, me_rows)
    picks = (relative[:, :, None] == jnp.arange(n_rows, dtype=jnp.int32)[None, None, :]) & is_live[:, :, None]
    sorted_rel = jnp.einsum(
        "tsq,tsab->tqab", picks.astype(jnp.bfloat16), values, preferred_element_type=jnp.bfloat16
    )
    sorted_rel = sorted_rel.reshape((panel_tiles,) + (2,) * nb + (tile, tile))

    if RADIX4_GATHER:
        held = radix_gather(features, n_rows)
        every = sorted_rel.reshape(panel_tiles, n_rows, tile, tile)
        partial_value = jnp.einsum(
            "tqab,qbf->taf", every, held.reshape(n_rows, block_rows, feat_width),
            preferred_element_type=jnp.float32,
        )
    else:
        down = list(range(nb - 1, -1, -1))
        gather_orders = [down, down[:-2] + [down[-1], down[-2]]][:GATHER_PARTS] if nb >= 2 else [down]
        width = feat_width // len(gather_orders)
        partial_value = jnp.concatenate(
            [
                gather_contract(features[:, k * width:(k + 1) * width], sorted_rel, order, n_rows)
                for k, order in enumerate(gather_orders)
            ],
            axis=-1,
        )
    panel_sum = doubling_sum(partial_value, "rep", n_rep, rep_bits)
    aggregated = panel_sum.reshape(panel_tiles * tile, feat_width).astype(jnp.bfloat16)

    preact = jnp.dot(aggregated, weight, preferred_element_type=jnp.float32)
    sigmoid_part = jax.nn.sigmoid(preact)
    output = (preact * sigmoid_part).astype(jnp.bfloat16)
    output = lax.dynamic_slice_in_dim(output, me_rep * block_rows, block_rows, 0)
    grad_pre = (
        cotangent.astype(jnp.float32) * sigmoid_part * (1.0 + preact * (1.0 - sigmoid_part))
    ).astype(jnp.bfloat16)
    pulled = lax.dot_general(
        grad_pre, weight, (((1,), (1,)), ((), ())), preferred_element_type=jnp.float32
    ).astype(jnp.bfloat16)
    local_weight = lax.dot_general(
        aggregated, grad_pre, (((0,), (0,)), ((), ())), preferred_element_type=jnp.float32
    )

    slice_rows = feat_width // n_rep
    w_slice = lax.dynamic_slice_in_dim(local_weight, me_rep * slice_rows, slice_rows, 0)
    if not W_PACKED and not PAIRED_BACKWARD:
        w_order = list(range(2, nb)) + [0, 1] if nb >= 2 else list(range(nb))
        w_slice = doubling_sum(w_slice, "rows", n_rows, w_order)

    pulled_tiles = pulled.reshape(panel_tiles, tile, feat_width)
    flat_rel = sorted_rel.reshape(panel_tiles, n_rows, tile, tile)
    up = list(range(nb))
    scatter_orders = ([up, [up[1], up[0]] + up[2:]] if nb >= 2 else [up])[:SCATTER_PARTS]
    if RADIX4_SCATTER:
        scatter_orders = [None]
    width = feat_width // len(scatter_orders)
    pieces = []
    for k, order in enumerate(scatter_orders):
        products = jnp.einsum(
            "tqab,taf->qbf",
            flat_rel,
            pulled_tiles[:, :, k * width:(k + 1) * width],
            preferred_element_type=jnp.float32,
        )
        products = products.reshape((2,) * nb + (block_rows, width))
        if order is None and PAIRED_BACKWARD:
            piece, w_slice = paired_backward(products, w_slice, n_rows, jnp.bfloat16)
            pieces.append(piece)
            continue
        if order is None:
            pieces.append(radix_scatter(products, n_rows, jnp.bfloat16))
            continue
        extra = w_slice.reshape(-1, width) if (W_PACKED and k == 0) else None
        piece, extra = halving_scatter(products, order, n_rows, jnp.bfloat16, extra)
        if extra is not None:
            w_slice = extra.reshape(slice_rows, feat_width)
        pieces.append(piece)
    feature_grad = jnp.concatenate(pieces, axis=-1).astype(jnp.bfloat16)
    weight_grad = doubling_gather(w_slice, "rep", n_rep).reshape(feat_width, feat_width)
    return (output, weight_grad, feature_grad)


def solution(mesh):
    return jax.shard_map(
        local,
        mesh=mesh,
        in_specs=(
            P(("rows", "rep"), None),
            P("rows", None),
            P(),
            P("rows", "rep", None, None, None),
            P("rows", "rep", None),
            P("rows", "rep"),
        ),
        out_specs=(P(("rows", "rep"), None), P(), P(("rows", "rep"), None)),
        check_vma=False,
    )
```

```python
import jax
import jax.numpy as jnp
from jax import lax
from jax.sharding import PartitionSpec as P


def bit_count(n):
    return n.bit_length() - 1


def pairs_of(n, mask):
    return [(j, j ^ mask) for j in range(n)]


def bit_rounds(nb):
    rounds = []
    top = nb
    while top > 0:
        rounds.append(tuple(range(max(top - 2, 0), top)))
        top -= 2
    return rounds


def radix_gather(x, n):
    nb = bit_count(n)
    held = x.reshape((1,) * nb + x.shape)
    for bits in bit_rounds(nb):
        if len(bits) == 1:
            got = lax.ppermute(held, "rows", pairs_of(n, 1 << bits[0]))
            held = jnp.concatenate([held, got], axis=nb - 1 - bits[0])
            continue
        low, high = bits
        got_low = lax.ppermute(held, "rows", pairs_of(n, 1 << low))
        got_high = lax.ppermute(held, "rows", pairs_of(n, 1 << high))
        got_both = lax.ppermute(held, "rows", pairs_of(n, (1 << low) | (1 << high)))
        first = jnp.concatenate([held, got_low], axis=nb - 1 - low)
        second = jnp.concatenate([got_high, got_both], axis=nb - 1 - low)
        held = jnp.concatenate([first, second], axis=nb - 1 - high)
    return held


def scatter_round(cur, bits, n, send_dtype):
    lead = cur.ndim - 2
    if len(bits) == 1:
        keep = lax.index_in_dim(cur, 0, lead - 1, keepdims=False)
        send = lax.index_in_dim(cur, 1, lead - 1, keepdims=False)
        return keep + lax.ppermute(send.astype(send_dtype), "rows", pairs_of(n, 1 << bits[0])).astype(jnp.float32)
    low, high = bits

    def part(h, l):
        return lax.index_in_dim(lax.index_in_dim(cur, h, lead - 2, keepdims=False), l, lead - 2, keepdims=False)

    got_low = lax.ppermute(part(0, 1).astype(send_dtype), "rows", pairs_of(n, 1 << low))
    got_high = lax.ppermute(part(1, 0).astype(send_dtype), "rows", pairs_of(n, 1 << high))
    got_both = lax.ppermute(part(1, 1).astype(send_dtype), "rows", pairs_of(n, (1 << low) | (1 << high)))
    return part(0, 0) + (got_low.astype(jnp.float32) + got_high.astype(jnp.float32) + got_both.astype(jnp.float32))


def sum_round(w, bits, n):
    if len(bits) == 1:
        return w + lax.ppermute(w, "rows", pairs_of(n, 1 << bits[0]))
    low, high = bits
    got_low = lax.ppermute(w, "rows", pairs_of(n, 1 << low))
    got_high = lax.ppermute(w, "rows", pairs_of(n, 1 << high))
    got_both = lax.ppermute(w, "rows", pairs_of(n, (1 << low) | (1 << high)))
    return (w + got_low) + (got_high + got_both)


def paired_backward(rel, w, n, send_dtype):
    rounds = bit_rounds(bit_count(n))
    cur = rel
    for k, bits in enumerate(rounds[::-1]):
        cur = scatter_round(cur, bits, n, send_dtype)
        w = sum_round(w, rounds[k], n)
    return cur, w


def rep_sum(x, n):
    for b in range(bit_count(n)):
        x = x + lax.ppermute(x, "rep", pairs_of(n, 1 << b))
    return x


def rep_gather(x, n):
    me = lax.axis_index("rep")
    buf = x[None]
    for b in range(bit_count(n)):
        got = lax.ppermute(buf, "rep", pairs_of(n, 1 << b))
        low = ((me >> b) & 1) == 0
        buf = jnp.where(low, jnp.concatenate([buf, got]), jnp.concatenate([got, buf]))
    return buf


def local(features, cotangent, weight, tile_vals, tile_cols, tile_count):
    n_rows = lax.axis_size("rows")
    n_rep = lax.axis_size("rep")
    tile = tile_vals.shape[-1]
    slots = tile_vals.shape[2]
    panel_tiles = tile_vals.shape[0]
    block_rows = features.shape[0]
    feat_width = features.shape[1]
    nb = bit_count(n_rows)
    me_rep = lax.axis_index("rep")
    me_rows = lax.axis_index("rows")

    values = tile_vals[:, 0]
    columns = tile_cols[:, 0]
    filled = tile_count[:, 0]

    is_live = jnp.arange(slots, dtype=jnp.int32)[None, :] < filled[:, None]
    relative = jnp.bitwise_xor(columns, me_rows)
    picks = (relative[:, :, None] == jnp.arange(n_rows, dtype=jnp.int32)[None, None, :]) & is_live[:, :, None]
    sorted_rel = jnp.einsum(
        "tsq,tsab->tqab", picks.astype(jnp.bfloat16), values, preferred_element_type=jnp.bfloat16
    )

    held = radix_gather(features, n_rows).reshape(n_rows, block_rows, feat_width)
    partial_value = jnp.einsum("tqab,qbf->taf", sorted_rel, held, preferred_element_type=jnp.float32)
    aggregated = rep_sum(partial_value, n_rep).reshape(panel_tiles * tile, feat_width).astype(jnp.bfloat16)

    preact = jnp.dot(aggregated, weight, preferred_element_type=jnp.float32)
    sigmoid_part = jax.nn.sigmoid(preact)
    output = (preact * sigmoid_part).astype(jnp.bfloat16)
    output = lax.dynamic_slice_in_dim(output, me_rep * block_rows, block_rows, 0)
    grad_pre = (
        cotangent.astype(jnp.float32) * sigmoid_part * (1.0 + preact * (1.0 - sigmoid_part))
    ).astype(jnp.bfloat16)
    pulled = lax.dot_general(
        grad_pre, weight, (((1,), (1,)), ((), ())), preferred_element_type=jnp.float32
    ).astype(jnp.bfloat16)
    local_weight = lax.dot_general(
        aggregated, grad_pre, (((0,), (0,)), ((), ())), preferred_element_type=jnp.float32
    )

    slice_rows = feat_width // n_rep
    w_slice = lax.dynamic_slice_in_dim(local_weight, me_rep * slice_rows, slice_rows, 0)

    pulled_tiles = pulled.reshape(panel_tiles, tile, feat_width)
    products = jnp.einsum("tqab,taf->qbf", sorted_rel, pulled_tiles, preferred_element_type=jnp.float32)
    products = products.reshape((2,) * nb + (block_rows, feat_width))
    summed, w_slice = paired_backward(products, w_slice, n_rows, jnp.bfloat16)
    feature_grad = summed.astype(jnp.bfloat16)
    weight_grad = rep_gather(w_slice, n_rep).reshape(feat_width, feat_width)
    return (output, weight_grad, feature_grad)


def solution(mesh):
    return jax.shard_map(
        local,
        mesh=mesh,
        in_specs=(
            P(("rows", "rep"), None),
            P("rows", None),
            P(),
            P("rows", "rep", None, None, None),
            P("rows", "rep", None),
            P("rows", "rep"),
        ),
        out_specs=(P(("rows", "rep"), None), P(), P(("rows", "rep"), None)),
        check_vma=False,
    )
```

```python
import jax
import jax.numpy as jnp
from jax import lax
from jax.sharding import PartitionSpec as P


def bit_count(n):
    return n.bit_length() - 1


def pairs_of(n, mask):
    return [(j, j ^ mask) for j in range(n)]


def bit_rounds(nb):
    rounds = []
    top = nb
    while top > 0:
        rounds.append(tuple(range(max(top - 2, 0), top)))
        top -= 2
    return rounds


def radix_gather(x, n):
    nb = bit_count(n)
    held = x.reshape((1,) * nb + x.shape)
    for bits in bit_rounds(nb):
        if len(bits) == 1:
            got = lax.ppermute(held, "rows", pairs_of(n, 1 << bits[0]))
            held = jnp.concatenate([held, got], axis=nb - 1 - bits[0])
            continue
        low, high = bits
        got_low = lax.ppermute(held, "rows", pairs_of(n, 1 << low))
        got_high = lax.ppermute(held, "rows", pairs_of(n, 1 << high))
        got_both = lax.ppermute(held, "rows", pairs_of(n, (1 << low) | (1 << high)))
        first = jnp.concatenate([held, got_low], axis=nb - 1 - low)
        second = jnp.concatenate([got_high, got_both], axis=nb - 1 - low)
        held = jnp.concatenate([first, second], axis=nb - 1 - high)
    return held


def scatter_round(cur, bits, n, send_dtype):
    lead = cur.ndim - 2
    if len(bits) == 1:
        keep = lax.index_in_dim(cur, 0, lead - 1, keepdims=False)
        send = lax.index_in_dim(cur, 1, lead - 1, keepdims=False)
        return keep + lax.ppermute(send.astype(send_dtype), "rows", pairs_of(n, 1 << bits[0])).astype(jnp.float32)
    low, high = bits

    def part(h, l):
        return lax.index_in_dim(lax.index_in_dim(cur, h, lead - 2, keepdims=False), l, lead - 2, keepdims=False)

    got_low = lax.ppermute(part(0, 1).astype(send_dtype), "rows", pairs_of(n, 1 << low))
    got_high = lax.ppermute(part(1, 0).astype(send_dtype), "rows", pairs_of(n, 1 << high))
    got_both = lax.ppermute(part(1, 1).astype(send_dtype), "rows", pairs_of(n, (1 << low) | (1 << high)))
    return part(0, 0) + (got_low.astype(jnp.float32) + got_high.astype(jnp.float32) + got_both.astype(jnp.float32))


def sum_round(w, bits, n):
    if len(bits) == 1:
        return w + lax.ppermute(w, "rows", pairs_of(n, 1 << bits[0]))
    low, high = bits
    got_low = lax.ppermute(w, "rows", pairs_of(n, 1 << low))
    got_high = lax.ppermute(w, "rows", pairs_of(n, 1 << high))
    got_both = lax.ppermute(w, "rows", pairs_of(n, (1 << low) | (1 << high)))
    return (w + got_low) + (got_high + got_both)


def paired_backward(rel, w, n, send_dtype):
    nb = bit_count(n)
    cur = rel
    if nb == 4:
        pairs = [((0, 1), (3,)), ((2,), (2,)), ((3,), (0, 1))]
    else:
        rounds = bit_rounds(nb)
        pairs = list(zip(rounds[::-1], rounds))
    for fg_bits, w_bits in pairs:
        cur = scatter_round(cur, fg_bits, n, send_dtype)
        w = sum_round(w, w_bits, n)
    return cur, w


def rep_sum(x, n):
    for b in range(bit_count(n)):
        x = x + lax.ppermute(x, "rep", pairs_of(n, 1 << b))
    return x


def rep_gather(x, n):
    me = lax.axis_index("rep")
    buf = x[None]
    for b in range(bit_count(n)):
        got = lax.ppermute(buf, "rep", pairs_of(n, 1 << b))
        low = ((me >> b) & 1) == 0
        buf = jnp.where(low, jnp.concatenate([buf, got]), jnp.concatenate([got, buf]))
    return buf


def local(features, cotangent, weight, tile_vals, tile_cols, tile_count):
    n_rows = lax.axis_size("rows")
    n_rep = lax.axis_size("rep")
    tile = tile_vals.shape[-1]
    slots = tile_vals.shape[2]
    panel_tiles = tile_vals.shape[0]
    block_rows = features.shape[0]
    feat_width = features.shape[1]
    nb = bit_count(n_rows)
    me_rep = lax.axis_index("rep")
    me_rows = lax.axis_index("rows")

    values = tile_vals[:, 0]
    columns = tile_cols[:, 0]
    filled = tile_count[:, 0]

    is_live = jnp.arange(slots, dtype=jnp.int32)[None, :] < filled[:, None]
    relative = jnp.bitwise_xor(columns, me_rows)
    picks = (relative[:, :, None] == jnp.arange(n_rows, dtype=jnp.int32)[None, None, :]) & is_live[:, :, None]
    sorted_rel = jnp.einsum(
        "tsq,tsab->tqab", picks.astype(jnp.bfloat16), values, preferred_element_type=jnp.bfloat16
    )

    held = radix_gather(features, n_rows).reshape(n_rows, block_rows, feat_width)
    partial_value = jnp.einsum("tqab,qbf->taf", sorted_rel, held, preferred_element_type=jnp.float32)
    aggregated = rep_sum(partial_value, n_rep).reshape(panel_tiles * tile, feat_width).astype(jnp.bfloat16)

    preact = jnp.dot(aggregated, weight, preferred_element_type=jnp.float32)
    sigmoid_part = jax.nn.sigmoid(preact)
    output = (preact * sigmoid_part).astype(jnp.bfloat16)
    output = lax.dynamic_slice_in_dim(output, me_rep * block_rows, block_rows, 0)
    grad_pre = (
        cotangent.astype(jnp.float32) * sigmoid_part * (1.0 + preact * (1.0 - sigmoid_part))
    ).astype(jnp.bfloat16)
    pulled = lax.dot_general(
        grad_pre, weight, (((1,), (1,)), ((), ())), preferred_element_type=jnp.float32
    ).astype(jnp.bfloat16)
    local_weight = lax.dot_general(
        aggregated, grad_pre, (((0,), (0,)), ((), ())), preferred_element_type=jnp.float32
    )

    slice_rows = feat_width // n_rep
    w_slice = lax.dynamic_slice_in_dim(local_weight, me_rep * slice_rows, slice_rows, 0)

    pulled_tiles = pulled.reshape(panel_tiles, tile, feat_width)
    products = jnp.einsum("tqab,taf->qbf", sorted_rel, pulled_tiles, preferred_element_type=jnp.float32)
    products = products.reshape((2,) * nb + (block_rows, feat_width))
    summed, w_slice = paired_backward(products, w_slice, n_rows, jnp.bfloat16)
    feature_grad = summed.astype(jnp.bfloat16)
    weight_grad = rep_gather(w_slice, n_rep).reshape(feat_width, feat_width)
    return (output, weight_grad, feature_grad)


def solution(mesh):
    return jax.shard_map(
        local,
        mesh=mesh,
        in_specs=(
            P(("rows", "rep"), None),
            P("rows", None),
            P(),
            P("rows", "rep", None, None, None),
            P("rows", "rep", None),
            P("rows", "rep"),
        ),
        out_specs=(P(("rows", "rep"), None), P(), P(("rows", "rep"), None)),
        check_vma=False,
    )
```

```python
import jax
import jax.numpy as jnp
from jax import lax
from jax.sharding import PartitionSpec as P


def bit_count(n):
    return n.bit_length() - 1


def pairs_of(n, mask):
    return [(j, j ^ mask) for j in range(n)]


def bit_rounds(nb):
    rounds = []
    top = nb
    while top > 0:
        rounds.append(tuple(range(max(top - 2, 0), top)))
        top -= 2
    return rounds


def radix_gather(x, n):
    nb = bit_count(n)
    held = x.reshape((1,) * nb + x.shape)
    for bits in bit_rounds(nb):
        if len(bits) == 1:
            got = lax.ppermute(held, "rows", pairs_of(n, 1 << bits[0]))
            held = jnp.concatenate([held, got], axis=nb - 1 - bits[0])
            continue
        low, high = bits
        got_low = lax.ppermute(held, "rows", pairs_of(n, 1 << low))
        got_high = lax.ppermute(held, "rows", pairs_of(n, 1 << high))
        got_both = lax.ppermute(held, "rows", pairs_of(n, (1 << low) | (1 << high)))
        first = jnp.concatenate([held, got_low], axis=nb - 1 - low)
        second = jnp.concatenate([got_high, got_both], axis=nb - 1 - low)
        held = jnp.concatenate([first, second], axis=nb - 1 - high)
    return held


def scatter_round(cur, bits, n, send_dtype):
    lead = cur.ndim - 2
    if len(bits) == 1:
        keep = lax.index_in_dim(cur, 0, lead - 1, keepdims=False)
        send = lax.index_in_dim(cur, 1, lead - 1, keepdims=False)
        return keep + lax.ppermute(send.astype(send_dtype), "rows", pairs_of(n, 1 << bits[0])).astype(jnp.float32)
    low, high = bits

    def part(h, l):
        return lax.index_in_dim(lax.index_in_dim(cur, h, lead - 2, keepdims=False), l, lead - 2, keepdims=False)

    got_low = lax.ppermute(part(0, 1).astype(send_dtype), "rows", pairs_of(n, 1 << low))
    got_high = lax.ppermute(part(1, 0).astype(send_dtype), "rows", pairs_of(n, 1 << high))
    got_both = lax.ppermute(part(1, 1).astype(send_dtype), "rows", pairs_of(n, (1 << low) | (1 << high)))
    return part(0, 0) + (got_low.astype(jnp.float32) + got_high.astype(jnp.float32) + got_both.astype(jnp.float32))


def sum_round(w, bits, n):
    if len(bits) == 1:
        return w + lax.ppermute(w, "rows", pairs_of(n, 1 << bits[0]))
    low, high = bits
    got_low = lax.ppermute(w, "rows", pairs_of(n, 1 << low))
    got_high = lax.ppermute(w, "rows", pairs_of(n, 1 << high))
    got_both = lax.ppermute(w, "rows", pairs_of(n, (1 << low) | (1 << high)))
    return (w + got_low) + (got_high + got_both)


def paired_backward(rel, w, n, send_dtype):
    nb = bit_count(n)
    cur = rel
    if nb == 4:
        pairs = [((0, 1), (3,)), ((2,), (2,)), ((3,), (0,)), (None, (1,))]
    else:
        rounds = bit_rounds(nb)
        pairs = list(zip(rounds[::-1], rounds))
    for fg_bits, w_bits in pairs:
        if fg_bits:
            cur = scatter_round(cur, fg_bits, n, send_dtype)
        if w_bits:
            w = sum_round(w, w_bits, n)
    return cur, w


def rep_sum(x, n):
    for b in range(bit_count(n)):
        x = x + lax.ppermute(x, "rep", pairs_of(n, 1 << b))
    return x


def rep_gather(x, n):
    me = lax.axis_index("rep")
    buf = x[None]
    for b in range(bit_count(n)):
        got = lax.ppermute(buf, "rep", pairs_of(n, 1 << b))
        low = ((me >> b) & 1) == 0
        buf = jnp.where(low, jnp.concatenate([buf, got]), jnp.concatenate([got, buf]))
    return buf


def local(features, cotangent, weight, tile_vals, tile_cols, tile_count):
    n_rows = lax.axis_size("rows")
    n_rep = lax.axis_size("rep")
    tile = tile_vals.shape[-1]
    slots = tile_vals.shape[2]
    panel_tiles = tile_vals.shape[0]
    block_rows = features.shape[0]
    feat_width = features.shape[1]
    nb = bit_count(n_rows)
    me_rep = lax.axis_index("rep")
    me_rows = lax.axis_index("rows")

    values = tile_vals[:, 0]
    columns = tile_cols[:, 0]
    filled = tile_count[:, 0]

    is_live = jnp.arange(slots, dtype=jnp.int32)[None, :] < filled[:, None]
    relative = jnp.bitwise_xor(columns, me_rows)
    picks = (relative[:, :, None] == jnp.arange(n_rows, dtype=jnp.int32)[None, None, :]) & is_live[:, :, None]
    sorted_rel = jnp.einsum(
        "tsq,tsab->tqab", picks.astype(jnp.bfloat16), values, preferred_element_type=jnp.bfloat16
    )

    held = radix_gather(features, n_rows).reshape(n_rows, block_rows, feat_width)
    partial_value = jnp.einsum("tqab,qbf->taf", sorted_rel, held, preferred_element_type=jnp.float32)
    aggregated = rep_sum(partial_value, n_rep).reshape(panel_tiles * tile, feat_width).astype(jnp.bfloat16)

    preact = jnp.dot(aggregated, weight, preferred_element_type=jnp.float32)
    sigmoid_part = jax.nn.sigmoid(preact)
    output = (preact * sigmoid_part).astype(jnp.bfloat16)
    output = lax.dynamic_slice_in_dim(output, me_rep * block_rows, block_rows, 0)
    grad_pre = (
        cotangent.astype(jnp.float32) * sigmoid_part * (1.0 + preact * (1.0 - sigmoid_part))
    ).astype(jnp.bfloat16)
    pulled = lax.dot_general(
        grad_pre, weight, (((1,), (1,)), ((), ())), preferred_element_type=jnp.float32
    ).astype(jnp.bfloat16)
    local_weight = lax.dot_general(
        aggregated, grad_pre, (((0,), (0,)), ((), ())), preferred_element_type=jnp.float32
    )

    slice_rows = feat_width // n_rep
    w_slice = lax.dynamic_slice_in_dim(local_weight, me_rep * slice_rows, slice_rows, 0)

    pulled_tiles = pulled.reshape(panel_tiles, tile, feat_width)
    products = jnp.einsum("tqab,taf->qbf", sorted_rel, pulled_tiles, preferred_element_type=jnp.float32)
    products = products.reshape((2,) * nb + (block_rows, feat_width))
    summed, w_slice = paired_backward(products, w_slice, n_rows, jnp.bfloat16)
    feature_grad = summed.astype(jnp.bfloat16)
    weight_grad = rep_gather(w_slice, n_rep).reshape(feat_width, feat_width)
    return (output, weight_grad, feature_grad)


def solution(mesh):
    return jax.shard_map(
        local,
        mesh=mesh,
        in_specs=(
            P(("rows", "rep"), None),
            P("rows", None),
            P(),
            P("rows", "rep", None, None, None),
            P("rows", "rep", None),
            P("rows", "rep"),
        ),
        out_specs=(P(("rows", "rep"), None), P(), P(("rows", "rep"), None)),
        check_vma=False,
    )
```
